512 devices in a mesh: leaf: 128 (over x, z, core), batch: 4 (over y).
Axes of the slice: x: 4, y: 4, z: 16, core: 2. Of those that a mesh axis runs over, the one named last changes fastest.
Arguments:
- pixels_low: int32 [1280, 512], P('leaf', 'batch'), may hold values from 0 to 255
- pixels_mid: int32 [512, 512], P('leaf', 'batch'), may hold values from 0 to 255
- pixels_top: int32 [128, 512], P('leaf', 'batch'), may hold values from 0 to 255
- emit_low: bfloat16 [1280, 256, 256], P('leaf'), may hold values from -153 to 0, as said below
- emit_mid: bfloat16 [512, 256, 256], P('leaf'), may hold values from -153 to 0, as said below
- emit_top: bfloat16 [128, 256, 256], P('leaf'), may hold values from -153 to 0, as said below
- trans_low: bfloat16 [1280, 256, 256], P('leaf'), may hold values from 0.0001171875 to 3.515625, as said below
- trans_mid: bfloat16 [512, 256, 256], P('leaf'), may hold values from 0.0001171875 to 3.515625, as said below
- outside_top: float32 [128, 512, 256], P('leaf', 'batch'), may hold values from -1708 to -292, as said below
- parent_low: int32 [1280], replicated, may hold values from 0 to 511, as said below
- parent_mid: int32 [512], replicated, may hold values from 0 to 127
Outputs:
- update_low: float32 [1280, 256, 256], P('leaf', 'batch')
- update_mid: float32 [512, 256, 256], P('leaf', 'batch')
The draws below stay inside these ranges and needn't reach their ends.
Inputs may be any that keep to these rules, and one draw needn't show every extreme that they name: `emit_low`: Log-probabilities of pixel values given a state. `emit_mid`: Log-probabilities of pixel values given a state. `emit_top`: Log-probabilities of pixel values given a state. `trans_low`: positive edge weights. `trans_mid`: positive edge weights. `outside_top`: Log-likelihood of the rest of the image given a state. `parent_low`: among the 10 bottom-level nodes of one leaf index, at most 3 have a parent p held by another leaf index (leaf index p // 4); some leaf index has exactly 3.
All inputs are finite; a program needn't handle non-finite values.
Results may differ from the reference program's by a relative error of at most 0.0015.
Values sent between devices are 32-bit elements; how exact they have to be, the bound alone decides.
No kernel may reach another device: no remote copies, remote signals or barrier semaphores. Data moves between devices by JAX's collectives and lax.ppermute only.
A program may use at most 64 MiB of HBM per device.

```python
import jax
import jax.numpy as jnp
from jax import lax

K = 256
V = 256
C0 = 10
C1 = 4
R0 = 3
B = 512
N0 = 1280
N1 = 512
N2 = 128


def emission_draw(key, count):
    keys = jax.random.split(key, 2)
    base = jax.random.uniform(keys[0], (count, V, 1), jnp.float32, -9.0, -3.0)
    noise = jax.random.uniform(keys[1], (count, V, K), jnp.float32, -3.0, 3.0)
    return (base + noise).astype(jnp.bfloat16)


def transition_draw(key, count):
    keys = jax.random.split(key, 1)
    states = jnp.arange(K, dtype=jnp.int32)
    diagonal = (states[:, None] == states[None, :]).astype(jnp.float32)
    values = jnp.exp(jax.random.uniform(keys[0], (count, K, K), jnp.float32, -1.5, 1.5))
    return (values * (1.0 + 32.0 * diagonal) / K).astype(jnp.bfloat16)


def draw_emit_low(key, part):
    return emission_draw(jax.random.fold_in(key, 11), N0)


def draw_emit_mid(key, part):
    return emission_draw(jax.random.fold_in(key, 12), N1)


def draw_emit_top(key, part):
    return emission_draw(jax.random.fold_in(key, 13), N2)


def draw_trans_low(key, part):
    return transition_draw(jax.random.fold_in(key, 21), N0)


def draw_trans_mid(key, part):
    return transition_draw(jax.random.fold_in(key, 22), N1)


def draw_outside_top(key, part):
    keys = jax.random.split(jax.random.fold_in(key, 31), 2)
    offset = jax.random.uniform(keys[0], (N2, B, 1), jnp.float32, -1600.0, -400.0)
    detail = jax.random.uniform(keys[1], (N2, B, K), jnp.float32, -4.0, 4.0)
    return offset + detail


def draw_parent_low(key, part):
    devices = N0 // C0
    keys = jax.random.split(jax.random.fold_in(key, 41), 5)
    owners_now = jnp.arange(devices, dtype=jnp.int32)[:, None]
    counts = jax.random.randint(keys[0], (devices,), R0 - R0 // 2, R0 + 1)
    forced = jax.random.randint(keys[1], (), 0, devices)
    counts = jnp.where(jnp.arange(devices, dtype=jnp.int32) == forced, R0, counts)
    scores = jax.random.randint(keys[2], (devices, C0), 0, 1 << 20) * C0 + jnp.arange(C0, dtype=jnp.int32)[None, :]
    ranks = jnp.argsort(jnp.argsort(scores, axis=1), axis=1)
    remote = ranks < counts[:, None]
    hops = jax.random.randint(keys[3], (devices, C0), 1, devices)
    owners = jnp.where(remote, (owners_now + hops) % devices, owners_now)
    slots = jax.random.randint(keys[4], (devices, C0), 0, C1)
    return (owners * C1 + slots).reshape(N0).astype(jnp.int32)


def set_ends(values, key, low, largest):
    longest = values.shape.index(max(values.shape))
    spots = []
    for shift in (0, 1):
        where = [jax.random.randint(jax.random.fold_in(key, axis), (), 0, length) for axis, length in enumerate(values.shape)]
        where[longest] = (where[longest] + shift) % values.shape[longest]
        spots.append(tuple(where))
    return values.at[spots[0]].set(low).at[spots[1]].set(largest)


def setup_inputs(seed: int = 0) -> dict:
    streams_of = jax.random.split(jax.random.key(seed), 12)
    return {
        "pixels_low": set_ends(jax.random.randint(streams_of[0], (N0, B), 0, V), jax.random.fold_in(streams_of[0], 1), 0, V - 1).astype(jnp.int32),
        "pixels_mid": set_ends(jax.random.randint(streams_of[1], (N1, B), 0, V), jax.random.fold_in(streams_of[1], 1), 0, V - 1).astype(jnp.int32),
        "pixels_top": set_ends(jax.random.randint(streams_of[2], (N2, B), 0, V), jax.random.fold_in(streams_of[2], 1), 0, V - 1).astype(jnp.int32),
        "emit_low": draw_emit_low(jax.random.fold_in(streams_of[11], 71), 0),
        "emit_mid": draw_emit_mid(jax.random.fold_in(streams_of[11], 71), 0),
        "emit_top": draw_emit_top(jax.random.fold_in(streams_of[11], 71), 0),
        "trans_low": draw_trans_low(jax.random.fold_in(streams_of[11], 71), 0),
        "trans_mid": draw_trans_mid(jax.random.fold_in(streams_of[11], 71), 0),
        "outside_top": draw_outside_top(jax.random.fold_in(streams_of[11], 71), 0),
        "parent_low": draw_parent_low(jax.random.fold_in(streams_of[11], 71), 0),
        "parent_mid": set_ends(jax.random.randint(streams_of[10], (N1,), 0, N2), jax.random.fold_in(streams_of[10], 1), 0, N2 - 1).astype(jnp.int32),
    }


PSEUDO = 0.001


def lookup(table, pixels):
    return jnp.take(table, pixels, axis=0).astype(jnp.float32)


def upward(inside, weight):
    top = jnp.max(inside, axis=-1, keepdims=True)
    scaled = jnp.exp(inside - top).astype(jnp.bfloat16)
    linear = jnp.dot(scaled, weight.T, preferred_element_type=jnp.float32)
    return jnp.log(linear) + top, scaled


def edge_update(above, weight, scaled):
    peak = jnp.max(above, axis=-1, keepdims=True)
    pushed = jnp.exp(above - peak).astype(jnp.bfloat16)
    reach = jnp.dot(pushed, weight, preferred_element_type=jnp.float32)
    total = jnp.sum(reach * scaled.astype(jnp.float32), axis=-1, keepdims=True)
    share = (pushed.astype(jnp.float32) / total).astype(jnp.bfloat16)
    counts = jnp.dot(share.T, scaled, preferred_element_type=jnp.float32) * weight.astype(jnp.float32) + PSEUDO
    update = K * counts / jnp.sum(counts, axis=-1, keepdims=True)
    return update, jnp.log(reach) + peak


def reference(pixels_low, pixels_mid, pixels_top, emit_low, emit_mid, emit_top, trans_low, trans_mid, outside_top, parent_low, parent_mid):
    def low_up(sums, item):
        table, weight, pixels, parent = item
        up_low, scaled = upward(lookup(table, pixels), weight)
        return sums.at[parent].add(up_low), None

    sums_mid, ignored = lax.scan(low_up, jnp.zeros((N1, B, K), jnp.float32), (emit_low, trans_low, pixels_low, parent_low))
    inside_mid = jax.vmap(lookup)(emit_mid, pixels_mid) + sums_mid
    up_mid, scaled_mid = lax.map(lambda item: upward(item[0], item[1]), (inside_mid, trans_mid))
    sums_top = jax.ops.segment_sum(up_mid, parent_mid, num_segments=N2)
    total_top = jax.vmap(lookup)(emit_top, pixels_top) + sums_top + outside_top
    above_mid = total_top[parent_mid] - up_mid
    update_mid, outside_mid = lax.map(lambda item: edge_update(item[0], item[1], item[2]), (above_mid, trans_mid, scaled_mid))
    total_mid = inside_mid + outside_mid

    def low_down(item):
        table, weight, pixels, parent = item
        up_low, scaled = upward(lookup(table, pixels), weight)
        above = lax.dynamic_index_in_dim(total_mid, parent, 0, keepdims=False) - up_low
        update, unused = edge_update(above, weight, scaled)
        return update

    update_low = lax.map(low_down, (emit_low, trans_low, pixels_low, parent_low))
    return update_low, update_mid
```

```python
import jax
import jax.numpy as jnp
from jax import lax
from jax.sharding import PartitionSpec as P

PSEUDO = 0.001
REMOTE = 3
HI = lax.Precision.HIGHEST


def lookup_all(table, pixels):
    levels = jnp.arange(table.shape[1], dtype=jnp.int32)
    picks = (pixels[:, :, None] == levels[None, None, :]).astype(jnp.bfloat16)
    return jnp.einsum("nbv,nvk->bnk", picks, table, preferred_element_type=jnp.float32)


def upward_all(inside, weight):
    top = jnp.max(inside, axis=-1, keepdims=True)
    scaled = jnp.exp(inside - top).astype(jnp.bfloat16)
    linear = jnp.einsum("bnj,nij->bni", scaled, weight, preferred_element_type=jnp.float32)
    return (jnp.log(linear) + top, scaled)


def edge_all(above, weight, scaled):
    peak = jnp.max(above, axis=-1, keepdims=True)
    pushed = jnp.exp(above - peak).astype(jnp.bfloat16)
    reach = jnp.einsum("bni,nij->bnj", pushed, weight, preferred_element_type=jnp.float32)
    total = jnp.sum(reach * scaled.astype(jnp.float32), axis=-1, keepdims=True)
    share = (pushed.astype(jnp.float32) / total).astype(jnp.bfloat16)
    counts = jnp.einsum("bni,bnj->nij", share, scaled, preferred_element_type=jnp.float32)
    return (counts * weight.astype(jnp.float32), jnp.log(reach) + peak)


def finish(summed):
    counts = summed + PSEUDO
    return counts.shape[-1] * counts / jnp.sum(counts, axis=-1, keepdims=True)


def pick(onehot, rows):
    return jnp.einsum("pq,qk->pk", onehot, rows, precision=HI, preferred_element_type=jnp.float32)


def swap(x):
    return lax.all_to_all(x, "leaf", split_axis=0, concat_axis=0, tiled=True)


def remote_slots(parent_low, devices, low_count, mid_count):
    owners = parent_low.reshape(devices, low_count)
    here = jnp.arange(devices, dtype=jnp.int32)[:, None]
    remote = (owners // mid_count) != here
    rank = jnp.cumsum(remote.astype(jnp.int32), axis=1) - 1
    slots = jnp.arange(REMOTE, dtype=jnp.int32)
    sel = remote[:, :, None] & (rank[:, :, None] == slots[None, None, :])
    dest = jnp.sum(jnp.where(sel, owners[:, :, None], 0), axis=1)
    valid = jnp.any(sel, axis=1)
    return sel, jnp.where(valid, dest, -1)


def body(
    pixels_low,
    pixels_mid,
    pixels_top,
    emit_low,
    emit_mid,
    emit_top,
    trans_low,
    trans_mid,
    outside_top,
    parent_low,
    parent_mid,
):
    devices = lax.axis_size("leaf")
    me = lax.axis_index("leaf")
    low_count = emit_low.shape[0]
    mid_count = emit_mid.shape[0]
    top_count = emit_top.shape[0]
    images = pixels_low.shape[1]
    k = emit_low.shape[2]
    f32 = jnp.float32

    sel_all, dest_all = remote_slots(parent_low, devices, low_count, mid_count)
    my_parents = lax.dynamic_slice_in_dim(parent_low, me * low_count, low_count)
    local_sel = my_parents[:, None] == (me * mid_count + jnp.arange(mid_count, dtype=jnp.int32))[None, :]
    my_remote = lax.dynamic_index_in_dim(sel_all, me, 0, keepdims=False)

    up_low, scaled_low = upward_all(lookup_all(emit_low, pixels_low), trans_low)
    emis_mid = lookup_all(emit_mid, pixels_mid)
    emis_top = lookup_all(emit_top, pixels_top)
    base_top = emis_top + jnp.transpose(outside_top, (1, 0, 2))

    local_sum = jnp.sum(jnp.where(local_sel[None, :, :, None], up_low[:, :, None, :], 0.0), axis=1)
    remote_msg = jnp.sum(jnp.where(my_remote[None, :, :, None], up_low[:, :, None, :], 0.0), axis=1)

    sent = swap(jnp.concatenate([remote_msg, base_top], axis=1))
    recv_remote = sent[:, :REMOTE, :].reshape(devices * REMOTE, k)
    recv_top = sent[:, REMOTE, :]

    mid_ids = jnp.arange(devices * mid_count, dtype=jnp.int32)
    to_mid = (dest_all.reshape(-1)[None, :] == mid_ids[:, None]).astype(f32)
    sums_remote = pick(to_mid, recv_remote)
    remote_sum = swap(sums_remote.reshape(devices, mid_count, k))

    inside_mid = emis_mid + local_sum + remote_sum
    up_mid, scaled_mid = upward_all(inside_mid, trans_mid)

    up_mid_all = swap(up_mid).reshape(devices * mid_count, k)
    top_ids = jnp.arange(devices * top_count, dtype=jnp.int32)
    to_top = (parent_mid[None, :] == top_ids[:, None]).astype(f32)
    total_top = recv_top.reshape(devices * top_count, k) + pick(to_top, up_mid_all)
    above_mid_img = pick(jnp.transpose(to_top), total_top) - up_mid_all
    above_mid = swap(above_mid_img.reshape(devices, mid_count, k))

    counts_mid, outside_mid = edge_all(above_mid, trans_mid, scaled_mid)
    update_mid = finish(lax.psum_scatter(counts_mid, "batch", scatter_dimension=1, tiled=True))
    total_mid = inside_mid + outside_mid

    total_mid_all = swap(total_mid).reshape(devices * mid_count, k)
    from_mid = jnp.transpose(to_mid)
    gathered = pick(from_mid, total_mid_all).reshape(devices, REMOTE, k)
    remote_total = swap(gathered)

    parent_total = jnp.sum(jnp.where(local_sel[None, :, :, None], total_mid[:, None, :, :], 0.0), axis=2)
    parent_total = parent_total + jnp.sum(
        jnp.where(my_remote[None, :, :, None], remote_total[:, None, :, :], 0.0), axis=2
    )
    counts_low, unused = edge_all(parent_total - up_low, trans_low, scaled_low)
    update_low = finish(lax.psum_scatter(counts_low, "batch", scatter_dimension=1, tiled=True))
    return (update_low, update_mid)


def solution(mesh):
    return jax.shard_map(
        body,
        mesh=mesh,
        in_specs=(
            P("leaf", "batch"),
            P("leaf", "batch"),
            P("leaf", "batch"),
            P("leaf", None, None),
            P("leaf", None, None),
            P("leaf", None, None),
            P("leaf", None, None),
            P("leaf", None, None),
            P("leaf", "batch", None),
            P(),
            P(),
        ),
        out_specs=(P("leaf", "batch", None), P("leaf", "batch", None)),
        check_vma=False,
    )
```

```python
import jax
import jax.numpy as jnp
from jax import lax
from jax.sharding import PartitionSpec as P

PSEUDO = 0.001
REMOTE = 3
HI = lax.Precision.HIGHEST


def lookup_all(table, pixels):
    levels = jnp.arange(table.shape[1], dtype=jnp.int32)
    picks = (pixels[:, :, None] == levels[None, None, :]).astype(jnp.bfloat16)
    return jnp.einsum("nbv,nvk->bnk", picks, table, preferred_element_type=jnp.float32)


def upward_all(inside, weight):
    top = jnp.max(inside, axis=-1, keepdims=True)
    scaled = jnp.exp(inside - top).astype(jnp.bfloat16)
    linear = jnp.einsum("bnj,nij->bni", scaled, weight, preferred_element_type=jnp.float32)
    return (jnp.log(linear) + top, scaled)


def edge_all(above, weight, scaled):
    peak = jnp.max(above, axis=-1, keepdims=True)
    pushed = jnp.exp(above - peak).astype(jnp.bfloat16)
    reach = jnp.einsum("bni,nij->bnj", pushed, weight, preferred_element_type=jnp.float32)
    total = jnp.sum(reach * scaled.astype(jnp.float32), axis=-1, keepdims=True)
    share = (pushed.astype(jnp.float32) / total).astype(jnp.bfloat16)
    counts = jnp.einsum("bni,bnj->nij", share, scaled, preferred_element_type=jnp.float32)
    return (counts * weight.astype(jnp.float32), jnp.log(reach) + peak)


def finish(summed):
    counts = summed + PSEUDO
    return counts.shape[-1] * counts / jnp.sum(counts, axis=-1, keepdims=True)


def pick(onehot, rows):
    return jnp.einsum("pq,qk->pk", onehot, rows, precision=HI, preferred_element_type=jnp.float32)


def swap(x):
    return lax.all_to_all(x, "leaf", split_axis=0, concat_axis=0, tiled=True)


def remote_slots(parent_low, devices, low_count, mid_count):
    owners = parent_low.reshape(devices, low_count)
    here = jnp.arange(devices, dtype=jnp.int32)[:, None]
    remote = (owners // mid_count) != here
    rank = jnp.cumsum(remote.astype(jnp.int32), axis=1) - 1
    slots = jnp.arange(REMOTE, dtype=jnp.int32)
    sel = remote[:, :, None] & (rank[:, :, None] == slots[None, None, :])
    dest = jnp.sum(jnp.where(sel, owners[:, :, None], 0), axis=1)
    valid = jnp.any(sel, axis=1)
    return sel, jnp.where(valid, dest, -1)


def body(
    pixels_low,
    pixels_mid,
    pixels_top,
    emit_low,
    emit_mid,
    emit_top,
    trans_low,
    trans_mid,
    outside_top,
    parent_low,
    parent_mid,
):
    devices = lax.axis_size("leaf")
    me = lax.axis_index("leaf")
    low_count = emit_low.shape[0]
    mid_count = emit_mid.shape[0]
    top_count = emit_top.shape[0]
    images = pixels_low.shape[1]
    k = emit_low.shape[2]
    f32 = jnp.float32

    sel_all, dest_all = remote_slots(parent_low, devices, low_count, mid_count)
    my_parents = lax.dynamic_slice_in_dim(parent_low, me * low_count, low_count)
    local_sel = my_parents[:, None] == (me * mid_count + jnp.arange(mid_count, dtype=jnp.int32))[None, :]
    my_remote = lax.dynamic_index_in_dim(sel_all, me, 0, keepdims=False)

    up_low, scaled_low = upward_all(lookup_all(emit_low, pixels_low), trans_low)
    emis_mid = lookup_all(emit_mid, pixels_mid)
    emis_top = lookup_all(emit_top, pixels_top)
    base_top = emis_top + jnp.transpose(outside_top, (1, 0, 2))

    local_sum = jnp.sum(jnp.where(local_sel[None, :, :, None], up_low[:, :, None, :], 0.0), axis=1)
    remote_msg = jnp.sum(jnp.where(my_remote[None, :, :, None], up_low[:, :, None, :], 0.0), axis=1)

    sent = swap(jnp.concatenate([remote_msg, base_top], axis=1))
    recv_remote = sent[:, :REMOTE, :].reshape(devices * REMOTE, k)
    recv_top = sent[:, REMOTE, :]

    mid_ids = jnp.arange(devices * mid_count, dtype=jnp.int32)
    to_mid = (dest_all.reshape(-1)[None, :] == mid_ids[:, None]).astype(f32)
    sums_remote = pick(to_mid, recv_remote)
    remote_sum = swap(sums_remote.reshape(devices, mid_count, k))

    inside_mid = emis_mid + local_sum + remote_sum
    up_mid, scaled_mid = upward_all(inside_mid, trans_mid)

    up_mid_all = swap(up_mid).reshape(devices * mid_count, k)
    top_ids = jnp.arange(devices * top_count, dtype=jnp.int32)
    to_top = (parent_mid[None, :] == top_ids[:, None]).astype(f32)
    total_top = recv_top.reshape(devices * top_count, k) + pick(to_top, up_mid_all)
    above_mid_img = pick(jnp.transpose(to_top), total_top) - up_mid_all
    above_mid = swap(above_mid_img.reshape(devices, mid_count, k))

    counts_mid, outside_mid = edge_all(above_mid, trans_mid, scaled_mid)
    total_mid = inside_mid + outside_mid

    local_total = jnp.sum(jnp.where(local_sel[None, :, :, None], total_mid[:, None, :, :], 0.0), axis=2)
    counts_near, unused = edge_all(local_total - up_low, trans_low, scaled_low)
    total_mid, counts_near = lax.optimization_barrier((total_mid, counts_near))
    summed_near = lax.psum_scatter(counts_near, "batch", scatter_dimension=1, tiled=True)
    total_mid_all = swap(total_mid).reshape(devices * mid_count, k)
    from_mid = jnp.transpose(to_mid)
    gathered = pick(from_mid, total_mid_all).reshape(devices, REMOTE, k)
    gathered, summed_near = lax.optimization_barrier((gathered, summed_near))
    remote_total = swap(gathered)
    update_near = finish(summed_near)
    update_mid = finish(lax.psum_scatter(counts_mid, "batch", scatter_dimension=1, tiled=True))

    slot = jnp.transpose(my_remote)
    far_trans = jnp.sum(jnp.where(slot[:, :, None, None], trans_low[None], jnp.zeros((), trans_low.dtype)), axis=1)
    far_scaled = jnp.sum(jnp.where(slot[None, :, :, None], scaled_low[:, None], jnp.zeros((), scaled_low.dtype)), axis=2)
    far_up = jnp.sum(jnp.where(slot[None, :, :, None], up_low[:, None], 0.0), axis=2)
    counts_far, unused = edge_all(remote_total - far_up, far_trans, far_scaled)
    update_far = finish(lax.psum_scatter(counts_far, "batch", scatter_dimension=1, tiled=True))
    far_of = jnp.sum(jnp.where(my_remote[:, :, None, None], update_far[None], 0.0), axis=1)
    update_low = jnp.where(jnp.any(my_remote, axis=1)[:, None, None], far_of, update_near)
    return (update_low, update_mid)


def solution(mesh):
    return jax.shard_map(
        body,
        mesh=mesh,
        in_specs=(
            P("leaf", "batch"),
            P("leaf", "batch"),
            P("leaf", "batch"),
            P("leaf", None, None),
            P("leaf", None, None),
            P("leaf", None, None),
            P("leaf", None, None),
            P("leaf", None, None),
            P("leaf", "batch", None),
            P(),
            P(),
        ),
        out_specs=(P("leaf", "batch", None), P("leaf", "batch", None)),
        check_vma=False,
    )
```

```python
import jax
import jax.numpy as jnp
from jax import lax
from jax.sharding import PartitionSpec as P

PSEUDO = 0.001
REMOTE = 3
HI = lax.Precision.HIGHEST


def lookup_all(table, pixels):
    levels = jnp.arange(table.shape[1], dtype=jnp.int32)
    picks = (pixels[:, :, None] == levels[None, None, :]).astype(jnp.bfloat16)
    return jnp.einsum("nbv,nvk->bnk", picks, table, preferred_element_type=jnp.float32)


def upward_all(inside, weight):
    top = jnp.max(inside, axis=-1, keepdims=True)
    scaled = jnp.exp(inside - top).astype(jnp.bfloat16)
    linear = jnp.einsum("bnj,nij->bni", scaled, weight, preferred_element_type=jnp.float32)
    return (jnp.log(linear) + top, scaled)


def edge_all(above, weight, scaled):
    peak = jnp.max(above, axis=-1, keepdims=True)
    pushed = jnp.exp(above - peak).astype(jnp.bfloat16)
    reach = jnp.einsum("bni,nij->bnj", pushed, weight, preferred_element_type=jnp.float32)
    total = jnp.sum(reach * scaled.astype(jnp.float32), axis=-1, keepdims=True)
    share = (pushed.astype(jnp.float32) / total).astype(jnp.bfloat16)
    counts = jnp.einsum("bni,bnj->nij", share, scaled, preferred_element_type=jnp.float32)
    return (counts * weight.astype(jnp.float32), jnp.log(reach) + peak)


def finish(summed):
    counts = summed + PSEUDO
    return counts.shape[-1] * counts / jnp.sum(counts, axis=-1, keepdims=True)


def pick(onehot, rows):
    return jnp.einsum("pq,qk->pk", onehot, rows, precision=HI, preferred_element_type=jnp.float32)


def swap(x):
    return lax.all_to_all(x, "leaf", split_axis=0, concat_axis=0, tiled=True)


def scatter_sum(x):
    peers = lax.axis_size("batch")
    me = lax.axis_index("batch")
    blocks = x.reshape(x.shape[0], peers, x.shape[1] // peers, *x.shape[2:])
    total = lax.dynamic_index_in_dim(blocks, me, 1, keepdims=False)
    for shift in range(1, peers):
        part = lax.dynamic_index_in_dim(blocks, (me + shift) % peers, 1, keepdims=False)
        total = total + lax.ppermute(part, "batch", [(j, (j + shift) % peers) for j in range(peers)])
    return total


def remote_slots(parent_low, devices, low_count, mid_count):
    owners = parent_low.reshape(devices, low_count)
    here = jnp.arange(devices, dtype=jnp.int32)[:, None]
    remote = (owners // mid_count) != here
    rank = jnp.cumsum(remote.astype(jnp.int32), axis=1) - 1
    slots = jnp.arange(REMOTE, dtype=jnp.int32)
    sel = remote[:, :, None] & (rank[:, :, None] == slots[None, None, :])
    dest = jnp.sum(jnp.where(sel, owners[:, :, None], 0), axis=1)
    valid = jnp.any(sel, axis=1)
    return sel, jnp.where(valid, dest, -1)


def body(
    pixels_low,
    pixels_mid,
    pixels_top,
    emit_low,
    emit_mid,
    emit_top,
    trans_low,
    trans_mid,
    outside_top,
    parent_low,
    parent_mid,
):
    devices = lax.axis_size("leaf")
    me = lax.axis_index("leaf")
    low_count = emit_low.shape[0]
    mid_count = emit_mid.shape[0]
    top_count = emit_top.shape[0]
    images = pixels_low.shape[1]
    k = emit_low.shape[2]
    f32 = jnp.float32

    sel_all, dest_all = remote_slots(parent_low, devices, low_count, mid_count)
    my_parents = lax.dynamic_slice_in_dim(parent_low, me * low_count, low_count)
    local_sel = my_parents[:, None] == (me * mid_count + jnp.arange(mid_count, dtype=jnp.int32))[None, :]
    my_remote = lax.dynamic_index_in_dim(sel_all, me, 0, keepdims=False)

    up_low, scaled_low = upward_all(lookup_all(emit_low, pixels_low), trans_low)
    emis_mid = lookup_all(emit_mid, pixels_mid)
    emis_top = lookup_all(emit_top, pixels_top)
    base_top = emis_top + jnp.transpose(outside_top, (1, 0, 2))

    local_sum = jnp.sum(jnp.where(local_sel[None, :, :, None], up_low[:, :, None, :], 0.0), axis=1)
    remote_msg = jnp.sum(jnp.where(my_remote[None, :, :, None], up_low[:, :, None, :], 0.0), axis=1)

    sent = swap(jnp.concatenate([remote_msg, base_top], axis=1))
    recv_remote = sent[:, :REMOTE, :].reshape(devices * REMOTE, k)
    recv_top = sent[:, REMOTE, :]

    mid_ids = jnp.arange(devices * mid_count, dtype=jnp.int32)
    to_mid = (dest_all.reshape(-1)[None, :] == mid_ids[:, None]).astype(f32)
    sums_remote = pick(to_mid, recv_remote)
    remote_sum = swap(sums_remote.reshape(devices, mid_count, k))

    inside_mid = emis_mid + local_sum + remote_sum
    up_mid, scaled_mid = upward_all(inside_mid, trans_mid)

    up_mid_all = swap(up_mid).reshape(devices * mid_count, k)
    top_ids = jnp.arange(devices * top_count, dtype=jnp.int32)
    to_top = (parent_mid[None, :] == top_ids[:, None]).astype(f32)
    total_top = recv_top.reshape(devices * top_count, k) + pick(to_top, up_mid_all)
    above_mid_img = pick(jnp.transpose(to_top), total_top) - up_mid_all
    above_mid = swap(above_mid_img.reshape(devices, mid_count, k))

    counts_mid, outside_mid = edge_all(above_mid, trans_mid, scaled_mid)
    total_mid = inside_mid + outside_mid

    local_total = jnp.sum(jnp.where(local_sel[None, :, :, None], total_mid[:, None, :, :], 0.0), axis=2)
    counts_near, unused = edge_all(local_total - up_low, trans_low, scaled_low)
    total_mid, counts_near = lax.optimization_barrier((total_mid, counts_near))
    summed_near = lax.psum_scatter(counts_near, "batch", scatter_dimension=1, tiled=True)
    total_mid_all = swap(total_mid).reshape(devices * mid_count, k)
    from_mid = jnp.transpose(to_mid)
    gathered = pick(from_mid, total_mid_all).reshape(devices, REMOTE, k)
    gathered, summed_near = lax.optimization_barrier((gathered, summed_near))
    remote_total = swap(gathered)
    update_near = finish(summed_near)
    update_mid = finish(lax.psum_scatter(counts_mid, "batch", scatter_dimension=1, tiled=True))

    slot = jnp.transpose(my_remote)
    far_trans = jnp.sum(jnp.where(slot[:, :, None, None], trans_low[None], jnp.zeros((), trans_low.dtype)), axis=1)
    far_scaled = jnp.sum(jnp.where(slot[None, :, :, None], scaled_low[:, None], jnp.zeros((), scaled_low.dtype)), axis=2)
    far_up = jnp.sum(jnp.where(slot[None, :, :, None], up_low[:, None], 0.0), axis=2)
    counts_far, unused = edge_all(remote_total - far_up, far_trans, far_scaled)
    update_far = finish(scatter_sum(counts_far))
    far_of = jnp.sum(jnp.where(my_remote[:, :, None, None], update_far[None], 0.0), axis=1)
    update_low = jnp.where(jnp.any(my_remote, axis=1)[:, None, None], far_of, update_near)
    return (update_low, update_mid)


def solution(mesh):
    return jax.shard_map(
        body,
        mesh=mesh,
        in_specs=(
            P("leaf", "batch"),
            P("leaf", "batch"),
            P("leaf", "batch"),
            P("leaf", None, None),
            P("leaf", None, None),
            P("leaf", None, None),
            P("leaf", None, None),
            P("leaf", None, None),
            P("leaf", "batch", None),
            P(),
            P(),
        ),
        out_specs=(P("leaf", "batch", None), P("leaf", "batch", None)),
        check_vma=False,
    )
```

```python
import jax
import jax.numpy as jnp
from jax import lax
from jax.sharding import PartitionSpec as P

PSEUDO = 0.001
REMOTE = 3
HI = lax.Precision.HIGHEST


def lookup_all(table, pixels):
    levels = jnp.arange(table.shape[1], dtype=jnp.int32)
    picks = (pixels[:, :, None] == levels[None, None, :]).astype(jnp.bfloat16)
    return jnp.einsum("nbv,nvk->bnk", picks, table, preferred_element_type=jnp.float32)


def upward_all(inside, weight):
    top = jnp.max(inside, axis=-1, keepdims=True)
    scaled = jnp.exp(inside - top).astype(jnp.bfloat16)
    linear = jnp.einsum("bnj,nij->bni", scaled, weight, preferred_element_type=jnp.float32)
    return (jnp.log(linear) + top, scaled)


def edge_all(above, weight, scaled):
    peak = jnp.max(above, axis=-1, keepdims=True)
    pushed = jnp.exp(above - peak).astype(jnp.bfloat16)
    reach = jnp.einsum("bni,nij->bnj", pushed, weight, preferred_element_type=jnp.float32)
    total = jnp.sum(reach * scaled.astype(jnp.float32), axis=-1, keepdims=True)
    share = (pushed.astype(jnp.float32) / total).astype(jnp.bfloat16)
    counts = jnp.einsum("bni,bnj->nij", share, scaled, preferred_element_type=jnp.float32)
    return (counts * weight.astype(jnp.float32), jnp.log(reach) + peak)


def finish(summed):
    counts = summed + PSEUDO
    return counts.shape[-1] * counts / jnp.sum(counts, axis=-1, keepdims=True)


def pick(onehot, rows):
    return jnp.einsum("pq,qk->pk", onehot, rows, precision=HI, preferred_element_type=jnp.float32)


def swap(x):
    return lax.all_to_all(x, "leaf", split_axis=0, concat_axis=0, tiled=True)


def scatter_sum(x):
    peers = lax.axis_size("batch")
    me = lax.axis_index("batch")
    blocks = x.reshape(x.shape[0], peers, x.shape[1] // peers, *x.shape[2:])
    total = lax.dynamic_index_in_dim(blocks, me, 1, keepdims=False)
    for shift in range(1, peers):
        part = lax.dynamic_index_in_dim(blocks, (me + shift) % peers, 1, keepdims=False)
        total = total + lax.ppermute(part, "batch", [(j, (j + shift) % peers) for j in range(peers)])
    return total


def remote_slots(parent_low, devices, low_count, mid_count):
    owners = parent_low.reshape(devices, low_count)
    here = jnp.arange(devices, dtype=jnp.int32)[:, None]
    remote = (owners // mid_count) != here
    rank = jnp.cumsum(remote.astype(jnp.int32), axis=1) - 1
    slots = jnp.arange(REMOTE, dtype=jnp.int32)
    sel = remote[:, :, None] & (rank[:, :, None] == slots[None, None, :])
    dest = jnp.sum(jnp.where(sel, owners[:, :, None], 0), axis=1)
    valid = jnp.any(sel, axis=1)
    return sel, jnp.where(valid, dest, -1)


def body(
    pixels_low,
    pixels_mid,
    pixels_top,
    emit_low,
    emit_mid,
    emit_top,
    trans_low,
    trans_mid,
    outside_top,
    parent_low,
    parent_mid,
):
    devices = lax.axis_size("leaf")
    me = lax.axis_index("leaf")
    low_count = emit_low.shape[0]
    mid_count = emit_mid.shape[0]
    top_count = emit_top.shape[0]
    images = pixels_low.shape[1]
    k = emit_low.shape[2]
    f32 = jnp.float32

    sel_all, dest_all = remote_slots(parent_low, devices, low_count, mid_count)
    my_parents = lax.dynamic_slice_in_dim(parent_low, me * low_count, low_count)
    local_sel = my_parents[:, None] == (me * mid_count + jnp.arange(mid_count, dtype=jnp.int32))[None, :]
    my_remote = lax.dynamic_index_in_dim(sel_all, me, 0, keepdims=False)

    up_low, scaled_low = upward_all(lookup_all(emit_low, pixels_low), trans_low)
    emis_mid = lookup_all(emit_mid, pixels_mid)
    emis_top = lookup_all(emit_top, pixels_top)
    base_top = emis_top + jnp.transpose(outside_top, (1, 0, 2))

    local_sum = jnp.sum(jnp.where(local_sel[None, :, :, None], up_low[:, :, None, :], 0.0), axis=1)
    remote_msg = jnp.sum(jnp.where(my_remote[None, :, :, None], up_low[:, :, None, :], 0.0), axis=1)

    sent = swap(jnp.concatenate([remote_msg, base_top], axis=1))
    recv_remote = sent[:, :REMOTE, :].reshape(devices * REMOTE, k)
    recv_top = sent[:, REMOTE, :]

    mid_ids = jnp.arange(devices * mid_count, dtype=jnp.int32)
    to_mid = (dest_all.reshape(-1)[None, :] == mid_ids[:, None]).astype(f32)
    sums_remote = pick(to_mid, recv_remote)
    remote_sum = swap(sums_remote.reshape(devices, mid_count, k))

    inside_mid = emis_mid + local_sum + remote_sum
    up_mid, scaled_mid = upward_all(inside_mid, trans_mid)

    up_mid_all = swap(up_mid).reshape(devices * mid_count, k)
    top_ids = jnp.arange(devices * top_count, dtype=jnp.int32)
    to_top = (parent_mid[None, :] == top_ids[:, None]).astype(f32)
    total_top = recv_top.reshape(devices * top_count, k) + pick(to_top, up_mid_all)
    above_mid_img = pick(jnp.transpose(to_top), total_top) - up_mid_all
    above_mid = swap(above_mid_img.reshape(devices, mid_count, k))

    counts_mid, outside_mid = edge_all(above_mid, trans_mid, scaled_mid)
    total_mid = inside_mid + outside_mid

    total_mid_all = swap(total_mid).reshape(devices * mid_count, k)
    from_mid = jnp.transpose(to_mid)
    gathered = pick(from_mid, total_mid_all).reshape(devices, REMOTE, k)
    local_total = jnp.sum(jnp.where(local_sel[None, :, :, None], total_mid[:, None, :, :], 0.0), axis=2)
    counts_near, unused = edge_all(local_total - up_low, trans_low, scaled_low)
    gathered, counts_near, counts_mid = lax.optimization_barrier((gathered, counts_near, counts_mid))
    remote_total = swap(gathered)
    update_near = finish(lax.psum_scatter(counts_near, "batch", scatter_dimension=1, tiled=True))
    update_mid = finish(lax.psum_scatter(counts_mid, "batch", scatter_dimension=1, tiled=True))

    slot = jnp.transpose(my_remote)
    far_trans = jnp.sum(jnp.where(slot[:, :, None, None], trans_low[None], jnp.zeros((), trans_low.dtype)), axis=1)
    far_scaled = jnp.sum(jnp.where(slot[None, :, :, None], scaled_low[:, None], jnp.zeros((), scaled_low.dtype)), axis=2)
    far_up = jnp.sum(jnp.where(slot[None, :, :, None], up_low[:, None], 0.0), axis=2)
    counts_far, unused = edge_all(remote_total - far_up, far_trans, far_scaled)
    update_far = finish(scatter_sum(counts_far))
    far_of = jnp.sum(jnp.where(my_remote[:, :, None, None], update_far[None], 0.0), axis=1)
    update_low = jnp.where(jnp.any(my_remote, axis=1)[:, None, None], far_of, update_near)
    return (update_low, update_mid)


def solution(mesh):
    return jax.shard_map(
        body,
        mesh=mesh,
        in_specs=(
            P("leaf", "batch"),
            P("leaf", "batch"),
            P("leaf", "batch"),
            P("leaf", None, None),
            P("leaf", None, None),
            P("leaf", None, None),
            P("leaf", None, None),
            P("leaf", None, None),
            P("leaf", "batch", None),
            P(),
            P(),
        ),
        out_specs=(P("leaf", "batch", None), P("leaf", "batch", None)),
        check_vma=False,
    )
```

```python
import jax
import jax.numpy as jnp
from jax import lax
from jax.sharding import PartitionSpec as P

PSEUDO = 0.001
REMOTE = 3
HI = lax.Precision.HIGHEST


def lookup_all(table, pixels):
    levels = jnp.arange(table.shape[1], dtype=jnp.int32)
    picks = (pixels[:, :, None] == levels[None, None, :]).astype(jnp.bfloat16)
    return jnp.einsum("nbv,nvk->bnk", picks, table, preferred_element_type=jnp.float32)


def upward_all(inside, weight):
    top = jnp.max(inside, axis=-1, keepdims=True)
    scaled = jnp.exp(inside - top).astype(jnp.bfloat16)
    linear = jnp.einsum("bnj,nij->bni", scaled, weight, preferred_element_type=jnp.float32)
    return (jnp.log(linear) + top, scaled)


def edge_all(above, weight, scaled):
    peak = jnp.max(above, axis=-1, keepdims=True)
    pushed = jnp.exp(above - peak).astype(jnp.bfloat16)
    reach = jnp.einsum("bni,nij->bnj", pushed, weight, preferred_element_type=jnp.float32)
    total = jnp.sum(reach * scaled.astype(jnp.float32), axis=-1, keepdims=True)
    share = (pushed.astype(jnp.float32) / total).astype(jnp.bfloat16)
    counts = jnp.einsum("bni,bnj->nij", share, scaled, preferred_element_type=jnp.float32)
    return (counts * weight.astype(jnp.float32), jnp.log(reach) + peak)


def finish(summed):
    counts = summed + PSEUDO
    return counts.shape[-1] * counts / jnp.sum(counts, axis=-1, keepdims=True)


def pick(onehot, rows):
    return jnp.einsum("pq,qk->pk", onehot, rows, precision=HI, preferred_element_type=jnp.float32)


def swap(x):
    return lax.all_to_all(x, "leaf", split_axis=0, concat_axis=0, tiled=True)


def scatter_sum(x):
    peers = lax.axis_size("batch")
    me = lax.axis_index("batch")
    blocks = x.reshape(x.shape[0], peers, x.shape[1] // peers, *x.shape[2:])
    total = lax.dynamic_index_in_dim(blocks, me, 1, keepdims=False)
    for shift in range(1, peers):
        part = lax.dynamic_index_in_dim(blocks, (me + shift) % peers, 1, keepdims=False)
        total = total + lax.ppermute(part, "batch", [(j, (j + shift) % peers) for j in range(peers)])
    return total


def remote_slots(parent_low, devices, low_count, mid_count):
    owners = parent_low.reshape(devices, low_count)
    here = jnp.arange(devices, dtype=jnp.int32)[:, None]
    remote = (owners // mid_count) != here
    rank = jnp.cumsum(remote.astype(jnp.int32), axis=1) - 1
    slots = jnp.arange(REMOTE, dtype=jnp.int32)
    sel = remote[:, :, None] & (rank[:, :, None] == slots[None, None, :])
    dest = jnp.sum(jnp.where(sel, owners[:, :, None], 0), axis=1)
    valid = jnp.any(sel, axis=1)
    return sel, jnp.where(valid, dest, -1)


def body(
    pixels_low,
    pixels_mid,
    pixels_top,
    emit_low,
    emit_mid,
    emit_top,
    trans_low,
    trans_mid,
    outside_top,
    parent_low,
    parent_mid,
):
    devices = lax.axis_size("leaf")
    me = lax.axis_index("leaf")
    low_count = emit_low.shape[0]
    mid_count = emit_mid.shape[0]
    top_count = emit_top.shape[0]
    images = pixels_low.shape[1]
    k = emit_low.shape[2]
    f32 = jnp.float32

    sel_all, dest_all = remote_slots(parent_low, devices, low_count, mid_count)
    my_parents = lax.dynamic_slice_in_dim(parent_low, me * low_count, low_count)
    local_sel = my_parents[:, None] == (me * mid_count + jnp.arange(mid_count, dtype=jnp.int32))[None, :]
    my_remote = lax.dynamic_index_in_dim(sel_all, me, 0, keepdims=False)

    up_low, scaled_low = upward_all(lookup_all(emit_low, pixels_low), trans_low)
    emis_mid = lookup_all(emit_mid, pixels_mid)
    emis_top = lookup_all(emit_top, pixels_top)
    base_top = emis_top + jnp.transpose(outside_top, (1, 0, 2))

    local_sum = jnp.sum(jnp.where(local_sel[None, :, :, None], up_low[:, :, None, :], 0.0), axis=1)
    remote_msg = jnp.sum(jnp.where(my_remote[None, :, :, None], up_low[:, :, None, :], 0.0), axis=1)

    sent = swap(jnp.concatenate([remote_msg, base_top], axis=1))

    mid_dev = jnp.arange(devices, dtype=jnp.int32)[:, None] * mid_count + jnp.arange(mid_count, dtype=jnp.int32)[None, :]
    dest_pad = jnp.concatenate([dest_all, jnp.full((devices, 1), -1, jnp.int32)], axis=1)
    to_mid = (mid_dev[:, :, None, None] == dest_pad[None, None, :, :]).astype(f32)
    to_top = (parent_mid.reshape(devices, mid_count)[None, :, :] == jnp.arange(devices, dtype=jnp.int32)[:, None, None]).astype(f32)

    remote_sum = swap(jnp.einsum("dqsr,srk->dqk", to_mid, sent, precision=HI, preferred_element_type=f32))

    inside_mid = emis_mid + local_sum + remote_sum
    up_mid, scaled_mid = upward_all(inside_mid, trans_mid)

    up_mid_all = swap(up_mid)
    total_top = sent[:, REMOTE, :] + jnp.einsum("tsq,sqk->tk", to_top, up_mid_all, precision=HI, preferred_element_type=f32)
    above_mid_img = jnp.einsum("tsq,tk->sqk", to_top, total_top, precision=HI, preferred_element_type=f32) - up_mid_all
    above_mid = swap(above_mid_img)

    counts_mid, outside_mid = edge_all(above_mid, trans_mid, scaled_mid)
    total_mid = inside_mid + outside_mid
    total_mid, counts_mid = lax.optimization_barrier((total_mid, counts_mid))
    summed_mid = lax.psum_scatter(counts_mid, "batch", scatter_dimension=1, tiled=True)

    total_mid_all = swap(total_mid)
    gathered = jnp.einsum("dqsr,dqk->srk", to_mid[:, :, :, :REMOTE], total_mid_all, precision=HI, preferred_element_type=f32)
    local_total = jnp.sum(jnp.where(local_sel[None, :, :, None], total_mid[:, None, :, :], 0.0), axis=2)
    counts_near, unused = edge_all(local_total - up_low, trans_low, scaled_low)
    gathered, counts_near, summed_mid = lax.optimization_barrier((gathered, counts_near, summed_mid))
    summed_near = lax.psum_scatter(counts_near, "batch", scatter_dimension=1, tiled=True)
    remote_total = swap(gathered)
    update_near = finish(summed_near)
    update_mid = finish(summed_mid)

    slot = jnp.transpose(my_remote)
    far_trans = jnp.sum(jnp.where(slot[:, :, None, None], trans_low[None], jnp.zeros((), trans_low.dtype)), axis=1)
    far_scaled = jnp.sum(jnp.where(slot[None, :, :, None], scaled_low[:, None], jnp.zeros((), scaled_low.dtype)), axis=2)
    far_up = jnp.sum(jnp.where(slot[None, :, :, None], up_low[:, None], 0.0), axis=2)
    counts_far, unused = edge_all(remote_total - far_up, far_trans, far_scaled)
    update_far = finish(scatter_sum(counts_far))
    far_of = jnp.sum(jnp.where(my_remote[:, :, None, None], update_far[None], 0.0), axis=1)
    update_low = jnp.where(jnp.any(my_remote, axis=1)[:, None, None], far_of, update_near)
    return (update_low, update_mid)


def solution(mesh):
    return jax.shard_map(
        body,
        mesh=mesh,
        in_specs=(
            P("leaf", "batch"),
            P("leaf", "batch"),
            P("leaf", "batch"),
            P("leaf", None, None),
            P("leaf", None, None),
            P("leaf", None, None),
            P("leaf", None, None),
            P("leaf", None, None),
            P("leaf", "batch", None),
            P(),
            P(),
        ),
        out_specs=(P("leaf", "batch", None), P("leaf", "batch", None)),
        check_vma=False,
    )
```

```python
import jax
import jax.numpy as jnp
from jax import lax
from jax.sharding import PartitionSpec as P

PSEUDO = 0.001
REMOTE = 3
HI = lax.Precision.HIGHEST


def lookup_all(table, pixels):
    levels = jnp.arange(table.shape[1], dtype=jnp.int32)
    picks = (pixels[:, :, None] == levels[None, None, :]).astype(jnp.bfloat16)
    return jnp.einsum("nbv,nvk->bnk", picks, table, preferred_element_type=jnp.float32)


def upward_all(inside, weight):
    top = jnp.max(inside, axis=-1, keepdims=True)
    scaled = jnp.exp(inside - top).astype(jnp.bfloat16)
    linear = jnp.einsum("bnj,nij->bni", scaled, weight, preferred_element_type=jnp.float32)
    return (jnp.log(linear) + top, scaled)


def edge_all(above, weight, scaled):
    peak = jnp.max(above, axis=-1, keepdims=True)
    pushed = jnp.exp(above - peak).astype(jnp.bfloat16)
    reach = jnp.einsum("bni,nij->bnj", pushed, weight, preferred_element_type=jnp.float32)
    total = jnp.sum(reach * scaled.astype(jnp.float32), axis=-1, keepdims=True)
    share = (pushed.astype(jnp.float32) / total).astype(jnp.bfloat16)
    counts = jnp.einsum("bni,bnj->nij", share, scaled, preferred_element_type=jnp.float32)
    return (counts * weight.astype(jnp.float32), jnp.log(reach) + peak)


def finish(summed):
    counts = summed + PSEUDO
    return counts.shape[-1] * counts / jnp.sum(counts, axis=-1, keepdims=True)


def pick(onehot, rows):
    return jnp.einsum("pq,qk->pk", onehot, rows, precision=HI, preferred_element_type=jnp.float32)


def swap(x):
    return lax.all_to_all(x, "leaf", split_axis=0, concat_axis=0, tiled=True)


def scatter_sum(x):
    peers = lax.axis_size("batch")
    me = lax.axis_index("batch")
    blocks = x.reshape(x.shape[0], peers, x.shape[1] // peers, *x.shape[2:])
    total = lax.dynamic_index_in_dim(blocks, me, 1, keepdims=False)
    for shift in range(1, peers):
        part = lax.dynamic_index_in_dim(blocks, (me + shift) % peers, 1, keepdims=False)
        total = total + lax.ppermute(part, "batch", [(j, (j + shift) % peers) for j in range(peers)])
    return total


def remote_slots(parent_low, devices, low_count, mid_count):
    owners = parent_low.reshape(devices, low_count)
    here = jnp.arange(devices, dtype=jnp.int32)[:, None]
    remote = (owners // mid_count) != here
    rank = jnp.cumsum(remote.astype(jnp.int32), axis=1) - 1
    slots = jnp.arange(REMOTE, dtype=jnp.int32)
    sel = remote[:, :, None] & (rank[:, :, None] == slots[None, None, :])
    dest = jnp.sum(jnp.where(sel, owners[:, :, None], 0), axis=1)
    valid = jnp.any(sel, axis=1)
    return sel, jnp.where(valid, dest, -1)


def body(
    pixels_low,
    pixels_mid,
    pixels_top,
    emit_low,
    emit_mid,
    emit_top,
    trans_low,
    trans_mid,
    outside_top,
    parent_low,
    parent_mid,
):
    devices = lax.axis_size("leaf")
    me = lax.axis_index("leaf")
    low_count = emit_low.shape[0]
    mid_count = emit_mid.shape[0]
    top_count = emit_top.shape[0]
    images = pixels_low.shape[1]
    k = emit_low.shape[2]
    f32 = jnp.float32

    sel_all, dest_all = remote_slots(parent_low, devices, low_count, mid_count)
    my_parents = lax.dynamic_slice_in_dim(parent_low, me * low_count, low_count)
    local_sel = my_parents[:, None] == (me * mid_count + jnp.arange(mid_count, dtype=jnp.int32))[None, :]
    my_remote = lax.dynamic_index_in_dim(sel_all, me, 0, keepdims=False)

    up_low, scaled_low = upward_all(lookup_all(emit_low, pixels_low), trans_low)
    emis_mid = lookup_all(emit_mid, pixels_mid)
    emis_top = lookup_all(emit_top, pixels_top)
    base_top = emis_top + jnp.transpose(outside_top, (1, 0, 2))

    local_sum = jnp.sum(jnp.where(local_sel[None, :, :, None], up_low[:, :, None, :], 0.0), axis=1)
    remote_msg = jnp.sum(jnp.where(my_remote[None, :, :, None], up_low[:, :, None, :], 0.0), axis=1)

    sent = swap(jnp.concatenate([remote_msg, base_top], axis=1))

    mid_dev = jnp.arange(devices, dtype=jnp.int32)[:, None] * mid_count + jnp.arange(mid_count, dtype=jnp.int32)[None, :]
    dest_pad = jnp.concatenate([dest_all, jnp.full((devices, 1), -1, jnp.int32)], axis=1)
    to_mid = (mid_dev[:, :, None, None] == dest_pad[None, None, :, :]).astype(f32)
    to_top = (parent_mid.reshape(devices, mid_count)[None, :, :] == jnp.arange(devices, dtype=jnp.int32)[:, None, None]).astype(f32)

    remote_sum = swap(jnp.einsum("dqsr,srk->dqk", to_mid, sent, precision=HI, preferred_element_type=f32))

    inside_mid = emis_mid + local_sum + remote_sum
    up_mid, scaled_mid = upward_all(inside_mid, trans_mid)

    up_mid_all = swap(up_mid)
    total_top = sent[:, REMOTE, :] + jnp.einsum("tsq,sqk->tk", to_top, up_mid_all, precision=HI, preferred_element_type=f32)
    above_mid_img = jnp.einsum("tsq,tk->sqk", to_top, total_top, precision=HI, preferred_element_type=f32) - up_mid_all
    above_mid = swap(above_mid_img)

    counts_mid, outside_mid = edge_all(above_mid, trans_mid, scaled_mid)
    total_mid = inside_mid + outside_mid
    total_mid, counts_mid = lax.optimization_barrier((total_mid, counts_mid))

    total_mid_all = swap(total_mid)
    gathered = jnp.einsum("dqsr,dqk->srk", to_mid[:, :, :, :REMOTE], total_mid_all, precision=HI, preferred_element_type=f32)
    local_total = jnp.sum(jnp.where(local_sel[None, :, :, None], total_mid[:, None, :, :], 0.0), axis=2)
    counts_near, unused = edge_all(local_total - up_low, trans_low, scaled_low)
    summed_mid = scatter_sum(counts_mid)
    summed_near = scatter_sum(counts_near)
    gathered, summed_near, summed_mid = lax.optimization_barrier((gathered, summed_near, summed_mid))
    remote_total = swap(gathered)
    update_near = finish(summed_near)
    update_mid = finish(summed_mid)

    slot = jnp.transpose(my_remote)
    far_trans = jnp.sum(jnp.where(slot[:, :, None, None], trans_low[None], jnp.zeros((), trans_low.dtype)), axis=1)
    far_scaled = jnp.sum(jnp.where(slot[None, :, :, None], scaled_low[:, None], jnp.zeros((), scaled_low.dtype)), axis=2)
    far_up = jnp.sum(jnp.where(slot[None, :, :, None], up_low[:, None], 0.0), axis=2)
    counts_far, unused = edge_all(remote_total - far_up, far_trans, far_scaled)
    update_far = finish(scatter_sum(counts_far))
    far_of = jnp.sum(jnp.where(my_remote[:, :, None, None], update_far[None], 0.0), axis=1)
    update_low = jnp.where(jnp.any(my_remote, axis=1)[:, None, None], far_of, update_near)
    return (update_low, update_mid)


def solution(mesh):
    return jax.shard_map(
        body,
        mesh=mesh,
        in_specs=(
            P("leaf", "batch"),
            P("leaf", "batch"),
            P("leaf", "batch"),
            P("leaf", None, None),
            P("leaf", None, None),
            P("leaf", None, None),
            P("leaf", None, None),
            P("leaf", None, None),
            P("leaf", "batch", None),
            P(),
            P(),
        ),
        out_specs=(P("leaf", "batch", None), P("leaf", "batch", None)),
        check_vma=False,
    )
```

```python
import jax
import jax.numpy as jnp
from jax import lax
from jax.sharding import PartitionSpec as P

PSEUDO = 0.001
REMOTE = 3
HI = lax.Precision.HIGHEST


def lookup_all(table, pixels):
    levels = jnp.arange(table.shape[1], dtype=jnp.int32)
    picks = (pixels[:, :, None] == levels[None, None, :]).astype(jnp.bfloat16)
    return jnp.einsum("nbv,nvk->bnk", picks, table, preferred_element_type=jnp.float32)


def upward_all(inside, weight):
    top = jnp.max(inside, axis=-1, keepdims=True)
    scaled = jnp.exp(inside - top).astype(jnp.bfloat16)
    linear = jnp.einsum("bnj,nij->bni", scaled, weight, preferred_element_type=jnp.float32)
    return (jnp.log(linear) + top, scaled)


def edge_all(above, weight, scaled):
    peak = jnp.max(above, axis=-1, keepdims=True)
    pushed = jnp.exp(above - peak).astype(jnp.bfloat16)
    reach = jnp.einsum("bni,nij->bnj", pushed, weight, preferred_element_type=jnp.float32)
    total = jnp.sum(reach * scaled.astype(jnp.float32), axis=-1, keepdims=True)
    share = (pushed.astype(jnp.float32) / total).astype(jnp.bfloat16)
    counts = jnp.einsum("bni,bnj->nij", share, scaled, preferred_element_type=jnp.float32)
    return (counts * weight.astype(jnp.float32), jnp.log(reach) + peak)


def finish(summed):
    counts = summed + PSEUDO
    return counts.shape[-1] * counts / jnp.sum(counts, axis=-1, keepdims=True)


def pick(onehot, rows):
    return jnp.einsum("pq,qk->pk", onehot, rows, precision=HI, preferred_element_type=jnp.float32)


def swap(x):
    return lax.all_to_all(x, "leaf", split_axis=0, concat_axis=0, tiled=True)


def scatter_sum(x):
    peers = lax.axis_size("batch")
    me = lax.axis_index("batch")
    blocks = x.reshape(x.shape[0], peers, x.shape[1] // peers, *x.shape[2:])
    total = lax.dynamic_index_in_dim(blocks, me, 1, keepdims=False)
    for shift in range(1, peers):
        part = lax.dynamic_index_in_dim(blocks, (me + shift) % peers, 1, keepdims=False)
        total = total + lax.ppermute(part, "batch", [(j, (j + shift) % peers) for j in range(peers)])
    return total


def remote_slots(parent_low, devices, low_count, mid_count):
    owners = parent_low.reshape(devices, low_count)
    here = jnp.arange(devices, dtype=jnp.int32)[:, None]
    remote = (owners // mid_count) != here
    rank = jnp.cumsum(remote.astype(jnp.int32), axis=1) - 1
    slots = jnp.arange(REMOTE, dtype=jnp.int32)
    sel = remote[:, :, None] & (rank[:, :, None] == slots[None, None, :])
    dest = jnp.sum(jnp.where(sel, owners[:, :, None], 0), axis=1)
    valid = jnp.any(sel, axis=1)
    return sel, jnp.where(valid, dest, -1)


def body(
    pixels_low,
    pixels_mid,
    pixels_top,
    emit_low,
    emit_mid,
    emit_top,
    trans_low,
    trans_mid,
    outside_top,
    parent_low,
    parent_mid,
):
    devices = lax.axis_size("leaf")
    me = lax.axis_index("leaf")
    low_count = emit_low.shape[0]
    mid_count = emit_mid.shape[0]
    top_count = emit_top.shape[0]
    images = pixels_low.shape[1]
    k = emit_low.shape[2]
    f32 = jnp.float32

    sel_all, dest_all = remote_slots(parent_low, devices, low_count, mid_count)
    my_parents = lax.dynamic_slice_in_dim(parent_low, me * low_count, low_count)
    local_sel = my_parents[:, None] == (me * mid_count + jnp.arange(mid_count, dtype=jnp.int32))[None, :]
    my_remote = lax.dynamic_index_in_dim(sel_all, me, 0, keepdims=False)

    up_low, scaled_low = upward_all(lookup_all(emit_low, pixels_low), trans_low)
    emis_mid = lookup_all(emit_mid, pixels_mid)
    emis_top = lookup_all(emit_top, pixels_top)
    base_top = emis_top + jnp.transpose(outside_top, (1, 0, 2))

    local_sum = jnp.sum(jnp.where(local_sel[None, :, :, None], up_low[:, :, None, :], 0.0), axis=1)
    remote_msg = jnp.sum(jnp.where(my_remote[None, :, :, None], up_low[:, :, None, :], 0.0), axis=1)

    sent = swap(jnp.concatenate([remote_msg, base_top], axis=1))

    mid_dev = jnp.arange(devices, dtype=jnp.int32)[:, None] * mid_count + jnp.arange(mid_count, dtype=jnp.int32)[None, :]
    dest_pad = jnp.concatenate([dest_all, jnp.full((devices, 1), -1, jnp.int32)], axis=1)
    to_mid = (mid_dev[:, :, None, None] == dest_pad[None, None, :, :]).astype(f32)
    to_top = (parent_mid.reshape(devices, mid_count)[None, :, :] == jnp.arange(devices, dtype=jnp.int32)[:, None, None]).astype(f32)

    remote_sum = swap(jnp.einsum("dqsr,srk->dqk", to_mid, sent, precision=HI, preferred_element_type=f32))

    inside_mid = emis_mid + local_sum + remote_sum
    up_mid, scaled_mid = upward_all(inside_mid, trans_mid)

    up_mid_all = swap(up_mid)
    total_top = sent[:, REMOTE, :] + jnp.einsum("tsq,sqk->tk", to_top, up_mid_all, precision=HI, preferred_element_type=f32)
    above_mid_img = jnp.einsum("tsq,tk->sqk", to_top, total_top, precision=HI, preferred_element_type=f32) - up_mid_all
    above_mid = swap(above_mid_img)

    counts_mid, outside_mid = edge_all(above_mid, trans_mid, scaled_mid)
    total_mid = inside_mid + outside_mid
    local_total = jnp.sum(jnp.where(local_sel[None, :, :, None], total_mid[:, None, :, :], 0.0), axis=2)
    counts_near, unused = edge_all(local_total - up_low, trans_low, scaled_low)
    total_mid, counts_near = lax.optimization_barrier((total_mid, counts_near))
    summed_near = lax.psum_scatter(counts_near, "batch", scatter_dimension=1, tiled=True)

    total_mid_all = swap(total_mid)
    gathered = jnp.einsum("dqsr,dqk->srk", to_mid[:, :, :, :REMOTE], total_mid_all, precision=HI, preferred_element_type=f32)
    gathered, summed_near = lax.optimization_barrier((gathered, summed_near))
    remote_total = swap(gathered)
    update_near = finish(summed_near)
    update_mid = finish(lax.psum_scatter(counts_mid, "batch", scatter_dimension=1, tiled=True))

    slot = jnp.transpose(my_remote)
    far_trans = jnp.sum(jnp.where(slot[:, :, None, None], trans_low[None], jnp.zeros((), trans_low.dtype)), axis=1)
    far_scaled = jnp.sum(jnp.where(slot[None, :, :, None], scaled_low[:, None], jnp.zeros((), scaled_low.dtype)), axis=2)
    far_up = jnp.sum(jnp.where(slot[None, :, :, None], up_low[:, None], 0.0), axis=2)
    counts_far, unused = edge_all(remote_total - far_up, far_trans, far_scaled)
    update_far = finish(scatter_sum(counts_far))
    far_of = jnp.sum(jnp.where(my_remote[:, :, None, None], update_far[None], 0.0), axis=1)
    update_low = jnp.where(jnp.any(my_remote, axis=1)[:, None, None], far_of, update_near)
    return (update_low, update_mid)


def solution(mesh):
    return jax.shard_map(
        body,
        mesh=mesh,
        in_specs=(
            P("leaf", "batch"),
            P("leaf", "batch"),
            P("leaf", "batch"),
            P("leaf", None, None),
            P("leaf", None, None),
            P("leaf", None, None),
            P("leaf", None, None),
            P("leaf", None, None),
            P("leaf", "batch", None),
            P(),
            P(),
        ),
        out_specs=(P("leaf", "batch", None), P("leaf", "batch", None)),
        check_vma=False,
    )
```

```python
import jax
import jax.numpy as jnp
from jax import lax
from jax.sharding import PartitionSpec as P

PSEUDO = 0.001
REMOTE = 3
HI = lax.Precision.HIGHEST


def lookup_all(table, pixels):
    levels = jnp.arange(table.shape[1], dtype=jnp.int32)
    picks = (pixels[:, :, None] == levels[None, None, :]).astype(jnp.bfloat16)
    return jnp.einsum("nbv,nvk->bnk", picks, table, preferred_element_type=jnp.float32)


def upward_all(inside, weight):
    top = jnp.max(inside, axis=-1, keepdims=True)
    scaled = jnp.exp(inside - top).astype(jnp.bfloat16)
    linear = jnp.einsum("bnj,nij->bni", scaled, weight, preferred_element_type=jnp.float32)
    return (jnp.log(linear) + top, scaled)


def edge_all(above, weight, scaled):
    peak = jnp.max(above, axis=-1, keepdims=True)
    pushed = jnp.exp(above - peak).astype(jnp.bfloat16)
    reach = jnp.einsum("bni,nij->bnj", pushed, weight, preferred_element_type=jnp.float32)
    total = jnp.sum(reach * scaled.astype(jnp.float32), axis=-1, keepdims=True)
    share = (pushed.astype(jnp.float32) / total).astype(jnp.bfloat16)
    counts = jnp.einsum("bni,bnj->nij", share, scaled, preferred_element_type=jnp.float32)
    return (counts * weight.astype(jnp.float32), jnp.log(reach) + peak)


def finish(summed):
    counts = summed + PSEUDO
    return counts.shape[-1] * counts / jnp.sum(counts, axis=-1, keepdims=True)


def pick(onehot, rows):
    return jnp.einsum("pq,qk->pk", onehot, rows, precision=HI, preferred_element_type=jnp.float32)


def swap(x):
    return lax.all_to_all(x, "leaf", split_axis=0, concat_axis=0, tiled=True)


def scatter_sum(x):
    peers = lax.axis_size("batch")
    me = lax.axis_index("batch")
    blocks = x.reshape(x.shape[0], peers, x.shape[1] // peers, *x.shape[2:])
    total = lax.dynamic_index_in_dim(blocks, me, 1, keepdims=False)
    for shift in range(1, peers):
        part = lax.dynamic_index_in_dim(blocks, (me + shift) % peers, 1, keepdims=False)
        total = total + lax.ppermute(part, "batch", [(j, (j + shift) % peers) for j in range(peers)])
    return total


def scatter_swap(x):
    peers = lax.axis_size("batch")
    blocks = x.reshape(x.shape[0], peers, x.shape[1] // peers, *x.shape[2:])
    blocks = jnp.moveaxis(blocks, 1, 0)
    return jnp.sum(lax.all_to_all(blocks, "batch", split_axis=0, concat_axis=0, tiled=True), axis=0)


def remote_slots(parent_low, devices, low_count, mid_count):
    owners = parent_low.reshape(devices, low_count)
    here = jnp.arange(devices, dtype=jnp.int32)[:, None]
    remote = (owners // mid_count) != here
    rank = jnp.cumsum(remote.astype(jnp.int32), axis=1) - 1
    slots = jnp.arange(REMOTE, dtype=jnp.int32)
    sel = remote[:, :, None] & (rank[:, :, None] == slots[None, None, :])
    dest = jnp.sum(jnp.where(sel, owners[:, :, None], 0), axis=1)
    valid = jnp.any(sel, axis=1)
    return sel, jnp.where(valid, dest, -1)


def body(
    pixels_low,
    pixels_mid,
    pixels_top,
    emit_low,
    emit_mid,
    emit_top,
    trans_low,
    trans_mid,
    outside_top,
    parent_low,
    parent_mid,
):
    devices = lax.axis_size("leaf")
    me = lax.axis_index("leaf")
    low_count = emit_low.shape[0]
    mid_count = emit_mid.shape[0]
    top_count = emit_top.shape[0]
    images = pixels_low.shape[1]
    k = emit_low.shape[2]
    f32 = jnp.float32

    sel_all, dest_all = remote_slots(parent_low, devices, low_count, mid_count)
    my_parents = lax.dynamic_slice_in_dim(parent_low, me * low_count, low_count)
    local_sel = my_parents[:, None] == (me * mid_count + jnp.arange(mid_count, dtype=jnp.int32))[None, :]
    my_remote = lax.dynamic_index_in_dim(sel_all, me, 0, keepdims=False)

    up_low, scaled_low = upward_all(lookup_all(emit_low, pixels_low), trans_low)
    emis_mid = lookup_all(emit_mid, pixels_mid)
    emis_top = lookup_all(emit_top, pixels_top)
    base_top = emis_top + jnp.transpose(outside_top, (1, 0, 2))

    local_sum = jnp.sum(jnp.where(local_sel[None, :, :, None], up_low[:, :, None, :], 0.0), axis=1)
    remote_msg = jnp.sum(jnp.where(my_remote[None, :, :, None], up_low[:, :, None, :], 0.0), axis=1)

    sent = swap(jnp.concatenate([remote_msg, base_top], axis=1))

    mid_dev = jnp.arange(devices, dtype=jnp.int32)[:, None] * mid_count + jnp.arange(mid_count, dtype=jnp.int32)[None, :]
    dest_pad = jnp.concatenate([dest_all, jnp.full((devices, 1), -1, jnp.int32)], axis=1)
    to_mid = (mid_dev[:, :, None, None] == dest_pad[None, None, :, :]).astype(f32)
    to_top = (parent_mid.reshape(devices, mid_count)[None, :, :] == jnp.arange(devices, dtype=jnp.int32)[:, None, None]).astype(f32)

    remote_sum = swap(jnp.einsum("dqsr,srk->dqk", to_mid, sent, precision=HI, preferred_element_type=f32))

    inside_mid = emis_mid + local_sum + remote_sum
    up_mid, scaled_mid = upward_all(inside_mid, trans_mid)

    up_mid_all = swap(up_mid)
    total_top = sent[:, REMOTE, :] + jnp.einsum("tsq,sqk->tk", to_top, up_mid_all, precision=HI, preferred_element_type=f32)
    above_mid_img = jnp.einsum("tsq,tk->sqk", to_top, total_top, precision=HI, preferred_element_type=f32) - up_mid_all
    above_mid = swap(above_mid_img)

    counts_mid, outside_mid = edge_all(above_mid, trans_mid, scaled_mid)
    total_mid = inside_mid + outside_mid
    local_total = jnp.sum(jnp.where(local_sel[None, :, :, None], total_mid[:, None, :, :], 0.0), axis=2)
    counts_near, unused = edge_all(local_total - up_low, trans_low, scaled_low)
    total_mid, counts_near = lax.optimization_barrier((total_mid, counts_near))
    summed_near = lax.psum_scatter(counts_near, "batch", scatter_dimension=1, tiled=True)

    total_mid_all = swap(total_mid)
    gathered = jnp.einsum("dqsr,dqk->srk", to_mid[:, :, :, :REMOTE], total_mid_all, precision=HI, preferred_element_type=f32)
    gathered, summed_near = lax.optimization_barrier((gathered, summed_near))
    remote_total = swap(gathered)
    update_near = finish(summed_near)
    update_mid = finish(lax.psum_scatter(counts_mid, "batch", scatter_dimension=1, tiled=True))

    slot = jnp.transpose(my_remote)
    far_trans = jnp.sum(jnp.where(slot[:, :, None, None], trans_low[None], jnp.zeros((), trans_low.dtype)), axis=1)
    far_scaled = jnp.sum(jnp.where(slot[None, :, :, None], scaled_low[:, None], jnp.zeros((), scaled_low.dtype)), axis=2)
    far_up = jnp.sum(jnp.where(slot[None, :, :, None], up_low[:, None], 0.0), axis=2)
    counts_far, unused = edge_all(remote_total - far_up, far_trans, far_scaled)
    update_far = finish(scatter_swap(counts_far))
    far_of = jnp.sum(jnp.where(my_remote[:, :, None, None], update_far[None], 0.0), axis=1)
    update_low = jnp.where(jnp.any(my_remote, axis=1)[:, None, None], far_of, update_near)
    return (update_low, update_mid)


def solution(mesh):
    return jax.shard_map(
        body,
        mesh=mesh,
        in_specs=(
            P("leaf", "batch"),
            P("leaf", "batch"),
            P("leaf", "batch"),
            P("leaf", None, None),
            P("leaf", None, None),
            P("leaf", None, None),
            P("leaf", None, None),
            P("leaf", None, None),
            P("leaf", "batch", None),
            P(),
            P(),
        ),
        out_specs=(P("leaf", "batch", None), P("leaf", "batch", None)),
        check_vma=False,
    )
```

```python
import jax
import jax.numpy as jnp
from jax import lax
from jax.sharding import PartitionSpec as P

PSEUDO = 0.001
REMOTE = 3
HI = lax.Precision.HIGHEST


def lookup_all(table, pixels):
    levels = jnp.arange(table.shape[1], dtype=jnp.int32)
    picks = (pixels[:, :, None] == levels[None, None, :]).astype(jnp.bfloat16)
    return jnp.einsum("nbv,nvk->bnk", picks, table, preferred_element_type=jnp.float32)


def upward_all(inside, weight):
    top = jnp.max(inside, axis=-1, keepdims=True)
    scaled = jnp.exp(inside - top).astype(jnp.bfloat16)
    linear = jnp.einsum("bnj,nij->bni", scaled, weight, preferred_element_type=jnp.float32)
    return (jnp.log(linear) + top, scaled)


def edge_all(above, weight, scaled):
    peak = jnp.max(above, axis=-1, keepdims=True)
    pushed = jnp.exp(above - peak).astype(jnp.bfloat16)
    reach = jnp.einsum("bni,nij->bnj", pushed, weight, preferred_element_type=jnp.float32)
    total = jnp.sum(reach * scaled.astype(jnp.float32), axis=-1, keepdims=True)
    share = (pushed.astype(jnp.float32) / total).astype(jnp.bfloat16)
    counts = jnp.einsum("bni,bnj->nij", share, scaled, preferred_element_type=jnp.float32)
    return (counts * weight.astype(jnp.float32), jnp.log(reach) + peak)


def finish(summed):
    counts = summed + PSEUDO
    return counts.shape[-1] * counts / jnp.sum(counts, axis=-1, keepdims=True)


def pick(onehot, rows):
    return jnp.einsum("pq,qk->pk", onehot, rows, precision=HI, preferred_element_type=jnp.float32)


def swap(x):
    return lax.all_to_all(x, "leaf", split_axis=0, concat_axis=0, tiled=True)


def scatter_sum(x):
    peers = lax.axis_size("batch")
    me = lax.axis_index("batch")
    blocks = x.reshape(x.shape[0], peers, x.shape[1] // peers, *x.shape[2:])
    total = lax.dynamic_index_in_dim(blocks, me, 1, keepdims=False)
    for shift in range(1, peers):
        part = lax.dynamic_index_in_dim(blocks, (me + shift) % peers, 1, keepdims=False)
        total = total + lax.ppermute(part, "batch", [(j, (j + shift) % peers) for j in range(peers)])
    return total


def scatter_swap(x):
    peers = lax.axis_size("batch")
    blocks = x.reshape(x.shape[0], peers, x.shape[1] // peers, *x.shape[2:])
    blocks = jnp.moveaxis(blocks, 1, 0)
    return jnp.sum(lax.all_to_all(blocks, "batch", split_axis=0, concat_axis=0, tiled=True), axis=0)


def remote_slots(parent_low, devices, low_count, mid_count):
    owners = parent_low.reshape(devices, low_count)
    here = jnp.arange(devices, dtype=jnp.int32)[:, None]
    remote = (owners // mid_count) != here
    rank = jnp.cumsum(remote.astype(jnp.int32), axis=1) - 1
    slots = jnp.arange(REMOTE, dtype=jnp.int32)
    sel = remote[:, :, None] & (rank[:, :, None] == slots[None, None, :])
    dest = jnp.sum(jnp.where(sel, owners[:, :, None], 0), axis=1)
    valid = jnp.any(sel, axis=1)
    return sel, jnp.where(valid, dest, -1)


def body(
    pixels_low,
    pixels_mid,
    pixels_top,
    emit_low,
    emit_mid,
    emit_top,
    trans_low,
    trans_mid,
    outside_top,
    parent_low,
    parent_mid,
):
    devices = lax.axis_size("leaf")
    me = lax.axis_index("leaf")
    low_count = emit_low.shape[0]
    mid_count = emit_mid.shape[0]
    top_count = emit_top.shape[0]
    images = pixels_low.shape[1]
    k = emit_low.shape[2]
    f32 = jnp.float32

    my_parents = lax.dynamic_slice_in_dim(parent_low, me * low_count, low_count)
    local_sel = my_parents[:, None] == (me * mid_count + jnp.arange(mid_count, dtype=jnp.int32))[None, :]
    remote_me = (my_parents // mid_count) != me
    rank_me = jnp.cumsum(remote_me.astype(jnp.int32)) - 1
    my_remote = remote_me[:, None] & (rank_me[:, None] == jnp.arange(REMOTE, dtype=jnp.int32)[None, :])

    up_low, scaled_low = upward_all(lookup_all(emit_low, pixels_low), trans_low)
    emis_mid = lookup_all(emit_mid, pixels_mid)
    emis_top = lookup_all(emit_top, pixels_top)
    base_top = emis_top + jnp.transpose(outside_top, (1, 0, 2))

    local_sum = jnp.sum(jnp.where(local_sel[None, :, :, None], up_low[:, :, None, :], 0.0), axis=1)
    remote_msg = jnp.sum(jnp.where(my_remote[None, :, :, None], up_low[:, :, None, :], 0.0), axis=1)

    sent = swap(jnp.concatenate([remote_msg, base_top], axis=1))
    unused, dest_all = remote_slots(parent_low, devices, low_count, mid_count)

    mid_dev = jnp.arange(devices, dtype=jnp.int32)[:, None] * mid_count + jnp.arange(mid_count, dtype=jnp.int32)[None, :]
    dest_pad = jnp.concatenate([dest_all, jnp.full((devices, 1), -1, jnp.int32)], axis=1)
    to_mid = (mid_dev[:, :, None, None] == dest_pad[None, None, :, :]).astype(f32)
    to_top = (parent_mid.reshape(devices, mid_count)[None, :, :] == jnp.arange(devices, dtype=jnp.int32)[:, None, None]).astype(f32)

    remote_sum = swap(jnp.einsum("dqsr,srk->dqk", to_mid, sent, precision=HI, preferred_element_type=f32))

    inside_mid = emis_mid + local_sum + remote_sum
    up_mid, scaled_mid = upward_all(inside_mid, trans_mid)

    up_mid_all = swap(up_mid)
    total_top = sent[:, REMOTE, :] + jnp.einsum("tsq,sqk->tk", to_top, up_mid_all, precision=HI, preferred_element_type=f32)
    above_mid_img = jnp.einsum("tsq,tk->sqk", to_top, total_top, precision=HI, preferred_element_type=f32) - up_mid_all
    above_mid = swap(above_mid_img)

    counts_mid, outside_mid = edge_all(above_mid, trans_mid, scaled_mid)
    total_mid = inside_mid + outside_mid
    local_total = jnp.sum(jnp.where(local_sel[None, :, :, None], total_mid[:, None, :, :], 0.0), axis=2)
    counts_near, unused = edge_all(local_total - up_low, trans_low, scaled_low)
    total_mid, counts_near = lax.optimization_barrier((total_mid, counts_near))
    summed_near = lax.psum_scatter(counts_near, "batch", scatter_dimension=1, tiled=True)

    total_mid_all = swap(total_mid)
    gathered = jnp.einsum("dqsr,dqk->srk", to_mid[:, :, :, :REMOTE], total_mid_all, precision=HI, preferred_element_type=f32)
    gathered, summed_near = lax.optimization_barrier((gathered, summed_near))
    remote_total = swap(gathered)
    update_near = finish(summed_near)
    update_mid = finish(lax.psum_scatter(counts_mid, "batch", scatter_dimension=1, tiled=True))

    slot = jnp.transpose(my_remote)
    far_trans = jnp.sum(jnp.where(slot[:, :, None, None], trans_low[None], jnp.zeros((), trans_low.dtype)), axis=1)
    far_scaled = jnp.sum(jnp.where(slot[None, :, :, None], scaled_low[:, None], jnp.zeros((), scaled_low.dtype)), axis=2)
    far_up = jnp.sum(jnp.where(slot[None, :, :, None], up_low[:, None], 0.0), axis=2)
    counts_far, unused = edge_all(remote_total - far_up, far_trans, far_scaled)
    update_far = finish(scatter_swap(counts_far))
    far_of = jnp.sum(jnp.where(my_remote[:, :, None, None], update_far[None], 0.0), axis=1)
    update_low = jnp.where(jnp.any(my_remote, axis=1)[:, None, None], far_of, update_near)
    return (update_low, update_mid)


def solution(mesh):
    return jax.shard_map(
        body,
        mesh=mesh,
        in_specs=(
            P("leaf", "batch"),
            P("leaf", "batch"),
            P("leaf", "batch"),
            P("leaf", None, None),
            P("leaf", None, None),
            P("leaf", None, None),
            P("leaf", None, None),
            P("leaf", None, None),
            P("leaf", "batch", None),
            P(),
            P(),
        ),
        out_specs=(P("leaf", "batch", None), P("leaf", "batch", None)),
        check_vma=False,
    )
```

```python
import jax
import jax.numpy as jnp
from jax import lax
from jax.sharding import PartitionSpec as P

PSEUDO = 0.001
REMOTE = 3
HI = lax.Precision.HIGHEST


def lookup_all(table, pixels):
    levels = jnp.arange(table.shape[1], dtype=jnp.int32)
    picks = (pixels[:, :, None] == levels[None, None, :]).astype(jnp.bfloat16)
    return jnp.einsum("nbv,nvk->bnk", picks, table, preferred_element_type=jnp.float32)


def upward_all(inside, weight):
    top = jnp.max(inside, axis=-1, keepdims=True)
    scaled = jnp.exp(inside - top).astype(jnp.bfloat16)
    linear = jnp.einsum("nbj,nij->nbi", jnp.swapaxes(scaled, 0, 1), weight, preferred_element_type=jnp.float32)
    linear = jnp.swapaxes(linear, 0, 1)
    return (jnp.log(linear) + top, scaled)


def edge_all(above, weight, scaled):
    peak = jnp.max(above, axis=-1, keepdims=True)
    pushed = jnp.exp(above - peak).astype(jnp.bfloat16)
    reach = jnp.einsum("nbi,nij->nbj", jnp.swapaxes(pushed, 0, 1), weight, preferred_element_type=jnp.float32)
    reach = jnp.swapaxes(reach, 0, 1)
    total = jnp.sum(reach * scaled.astype(jnp.float32), axis=-1, keepdims=True)
    share = (pushed.astype(jnp.float32) / total).astype(jnp.bfloat16)
    counts = jnp.einsum(
        "nbi,nbj->nij", jnp.swapaxes(share, 0, 1), jnp.swapaxes(scaled, 0, 1), preferred_element_type=jnp.float32
    )
    return (counts * weight.astype(jnp.float32), jnp.log(reach) + peak)


def finish(summed):
    counts = summed + PSEUDO
    return counts.shape[-1] * counts / jnp.sum(counts, axis=-1, keepdims=True)


def pick(onehot, rows):
    return jnp.einsum("pq,qk->pk", onehot, rows, precision=HI, preferred_element_type=jnp.float32)


def swap(x):
    return lax.all_to_all(x, "leaf", split_axis=0, concat_axis=0, tiled=True)


def scatter_sum(x):
    peers = lax.axis_size("batch")
    me = lax.axis_index("batch")
    blocks = x.reshape(x.shape[0], peers, x.shape[1] // peers, *x.shape[2:])
    total = lax.dynamic_index_in_dim(blocks, me, 1, keepdims=False)
    for shift in range(1, peers):
        part = lax.dynamic_index_in_dim(blocks, (me + shift) % peers, 1, keepdims=False)
        total = total + lax.ppermute(part, "batch", [(j, (j + shift) % peers) for j in range(peers)])
    return total


def scatter_swap(x):
    peers = lax.axis_size("batch")
    blocks = x.reshape(x.shape[0], peers, x.shape[1] // peers, *x.shape[2:])
    blocks = jnp.moveaxis(blocks, 1, 0)
    return jnp.sum(lax.all_to_all(blocks, "batch", split_axis=0, concat_axis=0, tiled=True), axis=0)


def remote_slots(parent_low, devices, low_count, mid_count):
    owners = parent_low.reshape(devices, low_count)
    here = jnp.arange(devices, dtype=jnp.int32)[:, None]
    remote = (owners // mid_count) != here
    rank = jnp.cumsum(remote.astype(jnp.int32), axis=1) - 1
    slots = jnp.arange(REMOTE, dtype=jnp.int32)
    sel = remote[:, :, None] & (rank[:, :, None] == slots[None, None, :])
    dest = jnp.sum(jnp.where(sel, owners[:, :, None], 0), axis=1)
    valid = jnp.any(sel, axis=1)
    return sel, jnp.where(valid, dest, -1)


def body(
    pixels_low,
    pixels_mid,
    pixels_top,
    emit_low,
    emit_mid,
    emit_top,
    trans_low,
    trans_mid,
    outside_top,
    parent_low,
    parent_mid,
):
    devices = lax.axis_size("leaf")
    me = lax.axis_index("leaf")
    low_count = emit_low.shape[0]
    mid_count = emit_mid.shape[0]
    top_count = emit_top.shape[0]
    images = pixels_low.shape[1]
    k = emit_low.shape[2]
    f32 = jnp.float32

    my_parents = lax.dynamic_slice_in_dim(parent_low, me * low_count, low_count)
    local_sel = my_parents[:, None] == (me * mid_count + jnp.arange(mid_count, dtype=jnp.int32))[None, :]
    remote_me = (my_parents // mid_count) != me
    rank_me = jnp.cumsum(remote_me.astype(jnp.int32)) - 1
    my_remote = remote_me[:, None] & (rank_me[:, None] == jnp.arange(REMOTE, dtype=jnp.int32)[None, :])

    up_low, scaled_low = upward_all(lookup_all(emit_low, pixels_low), trans_low)
    emis_mid = lookup_all(emit_mid, pixels_mid)
    emis_top = lookup_all(emit_top, pixels_top)
    base_top = emis_top + jnp.transpose(outside_top, (1, 0, 2))

    local_sum = jnp.sum(jnp.where(local_sel[None, :, :, None], up_low[:, :, None, :], 0.0), axis=1)
    remote_msg = jnp.sum(jnp.where(my_remote[None, :, :, None], up_low[:, :, None, :], 0.0), axis=1)

    sent = swap(jnp.concatenate([remote_msg, base_top], axis=1))
    unused, dest_all = remote_slots(parent_low, devices, low_count, mid_count)

    mid_dev = jnp.arange(devices, dtype=jnp.int32)[:, None] * mid_count + jnp.arange(mid_count, dtype=jnp.int32)[None, :]
    dest_pad = jnp.concatenate([dest_all, jnp.full((devices, 1), -1, jnp.int32)], axis=1)
    to_mid = (mid_dev[:, :, None, None] == dest_pad[None, None, :, :]).astype(f32)
    to_top = (parent_mid.reshape(devices, mid_count)[None, :, :] == jnp.arange(devices, dtype=jnp.int32)[:, None, None]).astype(f32)

    remote_sum = swap(jnp.einsum("dqsr,srk->dqk", to_mid, sent, precision=HI, preferred_element_type=f32))

    inside_mid = emis_mid + local_sum + remote_sum
    up_mid, scaled_mid = upward_all(inside_mid, trans_mid)

    up_mid_all = swap(up_mid)
    total_top = sent[:, REMOTE, :] + jnp.einsum("tsq,sqk->tk", to_top, up_mid_all, precision=HI, preferred_element_type=f32)
    above_mid_img = jnp.einsum("tsq,tk->sqk", to_top, total_top, precision=HI, preferred_element_type=f32) - up_mid_all
    above_mid = swap(above_mid_img)

    counts_mid, outside_mid = edge_all(above_mid, trans_mid, scaled_mid)
    total_mid = inside_mid + outside_mid
    local_total = jnp.sum(jnp.where(local_sel[None, :, :, None], total_mid[:, None, :, :], 0.0), axis=2)
    counts_near, unused = edge_all(local_total - up_low, trans_low, scaled_low)
    total_mid, counts_near = lax.optimization_barrier((total_mid, counts_near))
    summed_near = lax.psum_scatter(counts_near, "batch", scatter_dimension=1, tiled=True)

    total_mid_all = swap(total_mid)
    gathered = jnp.einsum("dqsr,dqk->srk", to_mid[:, :, :, :REMOTE], total_mid_all, precision=HI, preferred_element_type=f32)
    gathered, summed_near = lax.optimization_barrier((gathered, summed_near))
    remote_total = swap(gathered)
    update_near = finish(summed_near)
    update_mid = finish(lax.psum_scatter(counts_mid, "batch", scatter_dimension=1, tiled=True))

    slot = jnp.transpose(my_remote)
    far_trans = jnp.sum(jnp.where(slot[:, :, None, None], trans_low[None], jnp.zeros((), trans_low.dtype)), axis=1)
    far_scaled = jnp.sum(jnp.where(slot[None, :, :, None], scaled_low[:, None], jnp.zeros((), scaled_low.dtype)), axis=2)
    far_up = jnp.sum(jnp.where(slot[None, :, :, None], up_low[:, None], 0.0), axis=2)
    counts_far, unused = edge_all(remote_total - far_up, far_trans, far_scaled)
    update_far = finish(scatter_swap(counts_far))
    far_of = jnp.sum(jnp.where(my_remote[:, :, None, None], update_far[None], 0.0), axis=1)
    update_low = jnp.where(jnp.any(my_remote, axis=1)[:, None, None], far_of, update_near)
    return (update_low, update_mid)


def solution(mesh):
    return jax.shard_map(
        body,
        mesh=mesh,
        in_specs=(
            P("leaf", "batch"),
            P("leaf", "batch"),
            P("leaf", "batch"),
            P("leaf", None, None),
            P("leaf", None, None),
            P("leaf", None, None),
            P("leaf", None, None),
            P("leaf", None, None),
            P("leaf", "batch", None),
            P(),
            P(),
        ),
        out_specs=(P("leaf", "batch", None), P("leaf", "batch", None)),
        check_vma=False,
    )
```

```python
import jax
import jax.numpy as jnp
from jax import lax
from jax.sharding import PartitionSpec as P

PSEUDO = 0.001
REMOTE = 3
HI = lax.Precision.HIGHEST


def lookup_all(table, pixels):
    levels = jnp.arange(table.shape[1], dtype=jnp.int32)
    picks = (pixels[:, :, None] == levels[None, None, :]).astype(jnp.bfloat16)
    return jnp.einsum("nbv,nvk->bnk", picks, table, preferred_element_type=jnp.float32)


def upward_all(inside, weight):
    top = jnp.max(inside, axis=-1, keepdims=True)
    scaled = jnp.exp(inside - top).astype(jnp.bfloat16)
    linear = jnp.einsum("nbj,nij->nbi", jnp.swapaxes(scaled, 0, 1), weight, preferred_element_type=jnp.float32)
    linear = jnp.swapaxes(linear, 0, 1)
    return (jnp.log(linear) + top, scaled)


def edge_all(above, weight, scaled):
    peak = jnp.max(above, axis=-1, keepdims=True)
    pushed = jnp.exp(above - peak).astype(jnp.bfloat16)
    reach = jnp.einsum("nbi,nij->nbj", jnp.swapaxes(pushed, 0, 1), weight, preferred_element_type=jnp.float32)
    reach = jnp.swapaxes(reach, 0, 1)
    total = jnp.sum(reach * scaled.astype(jnp.float32), axis=-1, keepdims=True)
    share = (pushed.astype(jnp.float32) / total).astype(jnp.bfloat16)
    counts = jnp.einsum(
        "nbi,nbj->nij", jnp.swapaxes(share, 0, 1), jnp.swapaxes(scaled, 0, 1), preferred_element_type=jnp.float32
    )
    return (counts * weight.astype(jnp.float32), jnp.log(reach) + peak)


def finish(summed):
    counts = summed + PSEUDO
    return counts.shape[-1] * counts / jnp.sum(counts, axis=-1, keepdims=True)


def pick(onehot, rows):
    return jnp.einsum("pq,qk->pk", onehot, rows, precision=HI, preferred_element_type=jnp.float32)


def swap(x):
    return lax.all_to_all(x, "leaf", split_axis=0, concat_axis=0, tiled=True)


def scatter_sum(x):
    peers = lax.axis_size("batch")
    me = lax.axis_index("batch")
    blocks = x.reshape(x.shape[0], peers, x.shape[1] // peers, *x.shape[2:])
    total = lax.dynamic_index_in_dim(blocks, me, 1, keepdims=False)
    for shift in range(1, peers):
        part = lax.dynamic_index_in_dim(blocks, (me + shift) % peers, 1, keepdims=False)
        total = total + lax.ppermute(part, "batch", [(j, (j + shift) % peers) for j in range(peers)])
    return total


def scatter_swap(x):
    peers = lax.axis_size("batch")
    blocks = x.reshape(x.shape[0], peers, x.shape[1] // peers, *x.shape[2:])
    blocks = jnp.moveaxis(blocks, 1, 0)
    return jnp.sum(lax.all_to_all(blocks, "batch", split_axis=0, concat_axis=0, tiled=True), axis=0)


def remote_slots(parent_low, devices, low_count, mid_count):
    owners = parent_low.reshape(devices, low_count)
    here = jnp.arange(devices, dtype=jnp.int32)[:, None]
    remote = (owners // mid_count) != here
    rank = jnp.cumsum(remote.astype(jnp.int32), axis=1) - 1
    slots = jnp.arange(REMOTE, dtype=jnp.int32)
    sel = remote[:, :, None] & (rank[:, :, None] == slots[None, None, :])
    dest = jnp.sum(jnp.where(sel, owners[:, :, None], 0), axis=1)
    valid = jnp.any(sel, axis=1)
    return sel, jnp.where(valid, dest, -1)


def body(
    pixels_low,
    pixels_mid,
    pixels_top,
    emit_low,
    emit_mid,
    emit_top,
    trans_low,
    trans_mid,
    outside_top,
    parent_low,
    parent_mid,
):
    devices = lax.axis_size("leaf")
    me = lax.axis_index("leaf")
    low_count = emit_low.shape[0]
    mid_count = emit_mid.shape[0]
    top_count = emit_top.shape[0]
    images = pixels_low.shape[1]
    k = emit_low.shape[2]
    f32 = jnp.float32

    my_parents = lax.dynamic_slice_in_dim(parent_low, me * low_count, low_count)
    local_sel = my_parents[:, None] == (me * mid_count + jnp.arange(mid_count, dtype=jnp.int32))[None, :]
    remote_me = (my_parents // mid_count) != me
    rank_me = jnp.cumsum(remote_me.astype(jnp.int32)) - 1
    my_remote = remote_me[:, None] & (rank_me[:, None] == jnp.arange(REMOTE, dtype=jnp.int32)[None, :])

    up_low, scaled_low = upward_all(lookup_all(emit_low, pixels_low), trans_low)
    emis_mid = lookup_all(emit_mid, pixels_mid)
    emis_top = lookup_all(emit_top, pixels_top)
    base_top = emis_top + jnp.transpose(outside_top, (1, 0, 2))

    local_sum = jnp.sum(jnp.where(local_sel[None, :, :, None], up_low[:, :, None, :], 0.0), axis=1)
    remote_msg = jnp.sum(jnp.where(my_remote[None, :, :, None], up_low[:, :, None, :], 0.0), axis=1)

    sent = swap(jnp.concatenate([remote_msg, base_top], axis=1))
    unused, dest_all = remote_slots(parent_low, devices, low_count, mid_count)

    mid_dev = jnp.arange(devices, dtype=jnp.int32)[:, None] * mid_count + jnp.arange(mid_count, dtype=jnp.int32)[None, :]
    dest_pad = jnp.concatenate([dest_all, jnp.full((devices, 1), -1, jnp.int32)], axis=1)
    to_mid = (mid_dev[:, :, None, None] == dest_pad[None, None, :, :]).astype(f32)
    to_top = (parent_mid.reshape(devices, mid_count)[None, :, :] == jnp.arange(devices, dtype=jnp.int32)[:, None, None]).astype(f32)

    remote_sum = swap(jnp.einsum("dqsr,srk->dqk", to_mid, sent, precision=HI, preferred_element_type=f32))

    inside_mid = emis_mid + local_sum + remote_sum
    up_mid, scaled_mid = upward_all(inside_mid, trans_mid)

    up_mid_all = swap(up_mid)
    total_top = sent[:, REMOTE, :] + jnp.einsum("tsq,sqk->tk", to_top, up_mid_all, precision=HI, preferred_element_type=f32)
    above_mid_img = jnp.einsum("tsq,tk->sqk", to_top, total_top, precision=HI, preferred_element_type=f32) - up_mid_all
    above_mid = swap(above_mid_img)

    counts_mid, outside_mid = edge_all(above_mid, trans_mid, scaled_mid)
    total_mid = inside_mid + outside_mid
    local_total = jnp.sum(jnp.where(local_sel[None, :, :, None], total_mid[:, None, :, :], 0.0), axis=2)
    counts_near, unused = edge_all(local_total - up_low, trans_low, scaled_low)
    total_mid, counts_both = lax.optimization_barrier((total_mid, jnp.concatenate([counts_near, counts_mid], axis=0)))
    summed_both = lax.psum_scatter(counts_both, "batch", scatter_dimension=1, tiled=True)

    total_mid_all = swap(total_mid)
    gathered = jnp.einsum("dqsr,dqk->srk", to_mid[:, :, :, :REMOTE], total_mid_all, precision=HI, preferred_element_type=f32)
    gathered, summed_both = lax.optimization_barrier((gathered, summed_both))
    remote_total = swap(gathered)
    update_near = finish(summed_both[:low_count])
    update_mid = finish(summed_both[low_count:])

    slot = jnp.transpose(my_remote)
    far_trans = jnp.sum(jnp.where(slot[:, :, None, None], trans_low[None], jnp.zeros((), trans_low.dtype)), axis=1)
    far_scaled = jnp.sum(jnp.where(slot[None, :, :, None], scaled_low[:, None], jnp.zeros((), scaled_low.dtype)), axis=2)
    far_up = jnp.sum(jnp.where(slot[None, :, :, None], up_low[:, None], 0.0), axis=2)
    counts_far, unused = edge_all(remote_total - far_up, far_trans, far_scaled)
    update_far = finish(scatter_swap(counts_far))
    far_of = jnp.sum(jnp.where(my_remote[:, :, None, None], update_far[None], 0.0), axis=1)
    update_low = jnp.where(jnp.any(my_remote, axis=1)[:, None, None], far_of, update_near)
    return (update_low, update_mid)


def solution(mesh):
    return jax.shard_map(
        body,
        mesh=mesh,
        in_specs=(
            P("leaf", "batch"),
            P("leaf", "batch"),
            P("leaf", "batch"),
            P("leaf", None, None),
            P("leaf", None, None),
            P("leaf", None, None),
            P("leaf", None, None),
            P("leaf", None, None),
            P("leaf", "batch", None),
            P(),
            P(),
        ),
        out_specs=(P("leaf", "batch", None), P("leaf", "batch", None)),
        check_vma=False,
    )
```
